32 devices in a mesh: group: 2 (over x), seq: 16 (over z, y, core).
Axes of the slice: x: 2, y: 2, z: 4, core: 2. Of those that a mesh axis runs over, the one named last changes fastest.
Arguments:
- queries: bfloat16 [8192, 2048], P(('group', 'seq')), parts along dimension 0, may hold values from -200 to 200
- keys: bfloat16 [8192, 2048], P(('group', 'seq')), parts along dimension 0, may hold values from -7 to 7
- values: bfloat16 [8192, 2048], P(('group', 'seq')), parts along dimension 0, may hold values from -6 to 6
- grad_out: bfloat16 [8192, 2048], P(('group', 'seq')), parts along dimension 0, may hold values from -6 to 6
- view_mask: int32 [64, 4], P(('group', 'seq')), parts along dimension 0, may hold values 0 or 1
- tile_mask: int32 [64, 6], P(('group', 'seq')), parts along dimension 0, may hold values 0 or 1
Outputs:
- grad_queries: bfloat16 [8192, 2048], P(('group', 'seq')), parts along dimension 0
- grad_keys: bfloat16 [8192, 2048], P(('group', 'seq')), parts along dimension 0
- grad_values: bfloat16 [8192, 2048], P(('group', 'seq')), parts along dimension 0
The draws below stay inside these ranges and needn't reach their ends.
There are 2 independent parts, one for each index of `group`. The reference program is written for one: setup_inputs(seed, part) draws one part's arguments, and reference() takes and returns one part's arrays. A program takes and returns all parts, laid end to end along the dimension named above; each array names one. Nothing has to cross between parts.
All inputs are finite; a program needn't handle non-finite values. No bound on the sum of `view_mask` or of `tile_mask` on one device may be relied on, other than what follows from the above.
Results may differ from the reference program's by a relative error of at most 0.011.
Values may be sent and summed in bfloat16 or wider, within the bound.
No kernel may reach another device: no remote copies, remote signals or barrier semaphores. Data moves between devices by JAX's collectives and lax.ppermute only.
A program may use at most 128 MiB of HBM per device.

```python
import jax
import jax.numpy as jnp
from jax import lax

HEADS = 16
DH = 128
BLK = 128
CAMS = 4
TOK_DEV = 256
TOKENS = 4096
NBLK = 32
HD = 2048
N_SEQ = 16


def base_keys(key):
    return jax.random.truncated_normal(jax.random.fold_in(key, 7), -6.0, 6.0, (TOKENS, HEADS * DH), jnp.float32)


def draw_keys(key, part):
    drawn = base_keys(key)
    return drawn.astype(jnp.bfloat16)


def draw_queries(key, part):
    drawn = jax.random.truncated_normal(jax.random.fold_in(key, 3), -6.0, 6.0, (TOKENS, HEADS * DH), jnp.float32)
    return drawn.astype(jnp.bfloat16)


def plant(result, stream_key, least, top_value):
    longest = result.shape.index(max(result.shape))
    spots = []
    for shift in (0, 1):
        where = [jax.random.randint(jax.random.fold_in(stream_key, axis), (), 0, length) for axis, length in enumerate(result.shape)]
        where[longest] = (where[longest] + shift) % result.shape[longest]
        spots.append(tuple(where))
    return result.at[spots[0]].set(least).at[spots[1]].set(top_value)


def shard_levels(key, dims, cuts, least, high):
    gain = 1.0
    for axis_at, shards_of in cuts:
        draws = jax.random.uniform(jax.random.fold_in(jax.random.fold_in(key, 6), axis_at), (shards_of,), jnp.float32, least / len(cuts), high / len(cuts))
        gain = gain * jnp.repeat(jnp.exp(draws), dims[axis_at] // shards_of).reshape((-1,) + (1,) * (len(dims) - 1 - axis_at))
    return gain


def noise(key, dims, scale, most, cuts=(), held_as=jnp.bfloat16):
    result = jax.random.normal(key, dims, jnp.float32) * scale
    if len(cuts) > 0:
        result = shard_levels(key, dims, cuts, -0.22, 0.18) * result
    return jnp.clip(result, min=-most, max=most).astype(held_as)


def setup_inputs(seed: int = 0, part: int = 0) -> dict:
    arg_keys = jax.random.split(jax.random.key(seed), 7)
    part_splits = jax.random.split(jax.random.fold_in(arg_keys[6], part), 7)
    return {
        "queries": draw_queries(jax.random.fold_in(jax.random.fold_in(arg_keys[6], part), 71), part),
        "keys": draw_keys(jax.random.fold_in(jax.random.fold_in(arg_keys[6], part), 71), part),
        "values": noise(part_splits[2], (TOKENS, HD), 1.0, 6.0, ((0, 16),)),
        "grad_out": noise(part_splits[3], (TOKENS, HD), 1.0, 6.0, ((0, 16),)),
        "view_mask": plant((jax.random.randint(part_splits[4], (NBLK, 2 * (TOK_DEV // BLK)), 0, 3) < 1).astype(jnp.int32), jax.random.fold_in(part_splits[4], 1), 0, 1),
        "tile_mask": plant((jax.random.randint(part_splits[5], (NBLK, 3 * (TOK_DEV // BLK)), 0, 3) < 1).astype(jnp.int32), jax.random.fold_in(part_splits[5], 1), 0, 1),
    }


def block_allowed(view_rows, tile_rows, dev_blocks):
    joined = jnp.concatenate([view_rows[:, :dev_blocks], tile_rows, view_rows[:, dev_blocks:]], axis=1)
    block_count = joined.shape[0]
    own_column = 2 * dev_blocks + lax.broadcasted_iota(jnp.int32, (block_count, 5 * dev_blocks), 0) % dev_blocks
    column = lax.broadcasted_iota(jnp.int32, (block_count, 5 * dev_blocks), 1)
    return jnp.where(column == own_column, 1, joined)


def reference(queries, keys, values, grad_out, view_mask, tile_mask):
    dev_blocks = TOK_DEV // BLK
    camera_span = N_SEQ // CAMS
    shifts = (camera_span, 1, 0, -1, -camera_span)
    score_scale = DH ** -0.5
    feature_width = HEADS * DH

    def split_groups(array):
        return array.reshape(N_SEQ, TOK_DEV, feature_width)

    def beside_all(array):
        return jnp.concatenate([jnp.roll(array, offset, 0) for offset in shifts], axis=1)

    q_all = split_groups(queries)
    g_all = split_groups(grad_out)
    k_ctx = beside_all(split_groups(keys))
    v_ctx = beside_all(split_groups(values))
    blocks = block_allowed(view_mask, tile_mask, dev_blocks).reshape(N_SEQ, dev_blocks, 5 * dev_blocks)
    allowed = jnp.repeat(jnp.repeat(blocks, BLK, axis=1), BLK, axis=2) > 0

    def head_step(head_index, carry):
        grad_q, grad_k, grad_v = carry
        col_start = head_index * DH
        q_head = lax.dynamic_slice_in_dim(q_all, col_start, DH, 2).astype(jnp.float32)
        g_head = lax.dynamic_slice_in_dim(g_all, col_start, DH, 2).astype(jnp.float32)
        k_head = lax.dynamic_slice_in_dim(k_ctx, col_start, DH, 2).astype(jnp.float32)
        v_head = lax.dynamic_slice_in_dim(v_ctx, col_start, DH, 2).astype(jnp.float32)
        raw_scores = jnp.einsum("ntd,nud->ntu", q_head, k_head) * score_scale
        scores = jnp.where(allowed, raw_scores, -jnp.inf)
        row_top = jnp.max(scores, axis=2, keepdims=True)
        log_total = row_top + jnp.log(jnp.sum(jnp.exp(scores - row_top), axis=2, keepdims=True))
        prob_full = jnp.exp(scores - log_total)
        prob_half = lax.optimization_barrier(prob_full.astype(jnp.bfloat16)).astype(jnp.float32)
        attended = jnp.einsum("ntu,nud->ntd", prob_half, v_head)
        row_delta = jnp.sum(g_head * attended, axis=2, keepdims=True)
        grad_prob = jnp.einsum("ntd,nud->ntu", g_head, v_head)
        grad_score = lax.optimization_barrier((prob_full * (grad_prob - row_delta)).astype(jnp.bfloat16)).astype(jnp.float32)
        head_q = jnp.einsum("ntu,nud->ntd", grad_score, k_head) * score_scale
        head_k = jnp.einsum("ntu,ntd->nud", grad_score, q_head) * score_scale
        head_v = jnp.einsum("ntu,ntd->nud", prob_half, g_head)
        grad_q = lax.dynamic_update_slice_in_dim(grad_q, head_q, col_start, 2)
        grad_k = lax.dynamic_update_slice_in_dim(grad_k, head_k, col_start, 2)
        grad_v = lax.dynamic_update_slice_in_dim(grad_v, head_v, col_start, 2)
        return grad_q, grad_k, grad_v

    initial = (jnp.zeros((N_SEQ, TOK_DEV, feature_width), jnp.float32),
               jnp.zeros((N_SEQ, 5 * TOK_DEV, feature_width), jnp.float32),
               jnp.zeros((N_SEQ, 5 * TOK_DEV, feature_width), jnp.float32))
    grad_q, grad_k, grad_v = lax.fori_loop(0, HEADS, head_step, initial)

    def send_home(partials):
        pieces = partials.reshape(N_SEQ, 5, TOK_DEV, feature_width)
        pieces = lax.optimization_barrier(pieces.astype(jnp.bfloat16)).astype(jnp.float32)
        summed = pieces[:, 2]
        for slot_index in (0, 1, 3, 4):
            summed = summed + jnp.roll(pieces[:, slot_index], -shifts[slot_index], 0)
        return summed.reshape(TOKENS, feature_width).astype(jnp.bfloat16)

    return (grad_q.reshape(TOKENS, feature_width).astype(jnp.bfloat16), send_home(grad_k), send_home(grad_v))
```

```python
import jax
import jax.numpy as jnp
from jax import lax
from jax.sharding import PartitionSpec as P

DH = 128
BLK = 128
CAMS = 4
CHUNKS = 4


def from_behind(block, axis, distance):
    devices = range(lax.axis_size(axis))
    route = [((i - distance) % len(devices), i) for i in devices]
    return lax.ppermute(block, axis, route)


def block_allowed(view_rows, tile_rows, dev_blocks):
    joined = jnp.concatenate(
        [view_rows[:, :dev_blocks], tile_rows, view_rows[:, dev_blocks:]], axis=1
    )
    block_count = joined.shape[0]
    own_column = (
        2 * dev_blocks
        + lax.broadcasted_iota(jnp.int32, (block_count, 5 * dev_blocks), 0) % dev_blocks
    )
    column = lax.broadcasted_iota(jnp.int32, (block_count, 5 * dev_blocks), 1)
    return jnp.where(column == own_column, 1, joined)


def expand_blocks(blocks):
    row_blocks, col_blocks = blocks.shape
    spread = jnp.broadcast_to(blocks[:, None, :, None] > 0, (row_blocks, BLK, col_blocks, BLK))
    return spread.reshape(row_blocks * BLK, col_blocks * BLK)


def chunk_terms(q, k_ctx, v_ctx, g, allowed):
    score_scale = DH ** (-0.5)
    rows, width = q.shape
    heads = width // DH
    q3 = q.reshape(rows, heads, DH)
    g3 = g.reshape(rows, heads, DH)
    k3 = k_ctx.reshape(k_ctx.shape[0], heads, DH)
    v3 = v_ctx.reshape(v_ctx.shape[0], heads, DH)
    f32 = jnp.float32
    raw_scores = jnp.einsum("thd,uhd->htu", q3, k3, preferred_element_type=f32) * score_scale
    scores = jnp.where(allowed[None], raw_scores, -jnp.inf)
    row_top = jnp.max(scores, axis=2, keepdims=True)
    log_total = row_top + jnp.log(jnp.sum(jnp.exp(scores - row_top), axis=2, keepdims=True))
    prob_full = jnp.exp(scores - log_total)
    prob_half = prob_full.astype(jnp.bfloat16)
    attended = jnp.einsum("htu,uhd->thd", prob_half, v3, preferred_element_type=f32)
    row_delta = jnp.sum(g3.astype(f32) * attended, axis=2)
    grad_prob = jnp.einsum("thd,uhd->htu", g3, v3, preferred_element_type=f32)
    grad_score = (prob_full * (grad_prob - row_delta.T[:, :, None])).astype(jnp.bfloat16)
    head_q = jnp.einsum("htu,uhd->thd", grad_score, k3, preferred_element_type=f32) * score_scale
    head_k = jnp.einsum("htu,thd->uhd", grad_score, q3, preferred_element_type=f32) * score_scale
    head_v = jnp.einsum("htu,thd->uhd", prob_half, g3, preferred_element_type=f32)
    ctx_rows = k_ctx.shape[0]
    return (
        head_q.reshape(rows, width),
        head_k.reshape(ctx_rows, width),
        head_v.reshape(ctx_rows, width),
    )


def body(queries, keys, values, grad_out, view_mask, tile_mask):
    tok_rows, feature_width = queries.shape
    dev_blocks = tok_rows // BLK
    camera_span = lax.axis_size("seq") // CAMS
    shifts = (camera_span, 1, 0, -1, -camera_span)
    blocks = block_allowed(view_mask, tile_mask, dev_blocks)
    allowed = expand_blocks(blocks)
    chunk_width = feature_width // CHUNKS
    out_q, out_k, out_v = [], [], []
    for chunk in range(CHUNKS):
        low = chunk * chunk_width
        cols = slice(low, low + chunk_width)
        pair = jnp.stack([keys[:, cols], values[:, cols]])
        ctx = [pair if shift == 0 else from_behind(pair, "seq", shift) for shift in shifts]
        k_ctx = jnp.concatenate([c[0] for c in ctx], axis=0)
        v_ctx = jnp.concatenate([c[1] for c in ctx], axis=0)
        head_q, head_k, head_v = chunk_terms(
            queries[:, cols], k_ctx, v_ctx, grad_out[:, cols], allowed
        )
        half_k = head_k.astype(jnp.bfloat16).reshape(5, tok_rows, chunk_width)
        half_v = head_v.astype(jnp.bfloat16).reshape(5, tok_rows, chunk_width)
        summed_k = half_k[2].astype(jnp.float32)
        summed_v = half_v[2].astype(jnp.float32)
        for slot_index in (0, 1, 3, 4):
            back = from_behind(
                jnp.stack([half_k[slot_index], half_v[slot_index]]), "seq", -shifts[slot_index]
            )
            summed_k = summed_k + back[0].astype(jnp.float32)
            summed_v = summed_v + back[1].astype(jnp.float32)
        out_q.append(head_q.astype(jnp.bfloat16))
        out_k.append(summed_k.astype(jnp.bfloat16))
        out_v.append(summed_v.astype(jnp.bfloat16))
    return (
        jnp.concatenate(out_q, axis=1),
        jnp.concatenate(out_k, axis=1),
        jnp.concatenate(out_v, axis=1),
    )


def solution(mesh):
    placed = (
        P(("group", "seq"), None),
        P(("group", "seq"), None),
        P(("group", "seq"), None),
        P(("group", "seq"), None),
        P(("group", "seq"), None),
        P(("group", "seq"), None),
    )
    return jax.shard_map(
        body,
        mesh=mesh,
        in_specs=placed,
        out_specs=(P(("group", "seq"), None), P(("group", "seq"), None), P(("group", "seq"), None)),
        check_vma=False,
    )
```

```python
import functools

import jax
import jax.numpy as jnp
from jax import lax
from jax.experimental import pallas as pl
from jax.experimental.pallas import tpu as pltpu
from jax.sharding import PartitionSpec as P

DH = 128
BLK = 128
CAMS = 4
CHUNKS = 2
SLOTS = 5


def from_behind(block, axis, distance):
    devices = range(lax.axis_size(axis))
    route = [((i - distance) % len(devices), i) for i in devices]
    return lax.ppermute(block, axis, route)


def block_allowed(view_rows, tile_rows, dev_blocks):
    joined = jnp.concatenate(
        [view_rows[:, :dev_blocks], tile_rows, view_rows[:, dev_blocks:]], axis=1
    )
    block_count = joined.shape[0]
    own_column = (
        2 * dev_blocks
        + lax.broadcasted_iota(jnp.int32, (block_count, 5 * dev_blocks), 0) % dev_blocks
    )
    column = lax.broadcasted_iota(jnp.int32, (block_count, 5 * dev_blocks), 1)
    return jnp.where(column == own_column, 1, joined)


def expand_blocks(blocks):
    row_blocks, col_blocks = blocks.shape
    spread = jnp.broadcast_to(blocks[:, None, :, None], (row_blocks, BLK, col_blocks, BLK))
    return spread.reshape(row_blocks * BLK, col_blocks * BLK)


def head_kernel(mask_ref, q_ref, g_ref, *refs):
    kv_refs = refs[:SLOTS]
    dq_ref = refs[SLOTS]
    dkv_refs = refs[SLOTS + 1 :]
    f32 = jnp.float32
    score_scale = DH ** (-0.5)
    q = q_ref[...]
    g = g_ref[...]
    k = jnp.concatenate([r[0] for r in kv_refs], axis=0)
    v = jnp.concatenate([r[1] for r in kv_refs], axis=0)
    last = (((1,), (1,)), ((), ()))
    first = (((0,), (0,)), ((), ()))
    raw_scores = lax.dot_general(q, k, last, preferred_element_type=f32) * score_scale
    scores = jnp.where(mask_ref[...] > 0, raw_scores, -jnp.inf)
    row_top = jnp.max(scores, axis=1, keepdims=True)
    log_total = row_top + jnp.log(jnp.sum(jnp.exp(scores - row_top), axis=1, keepdims=True))
    prob_full = jnp.exp(scores - log_total)
    prob_half = prob_full.astype(jnp.bfloat16)
    attended = jnp.dot(prob_half, v, preferred_element_type=f32)
    row_delta = jnp.sum(g.astype(f32) * attended, axis=1, keepdims=True)
    grad_prob = lax.dot_general(g, v, last, preferred_element_type=f32)
    grad_score = (prob_full * (grad_prob - row_delta)).astype(jnp.bfloat16)
    dq_ref[...] = (jnp.dot(grad_score, k, preferred_element_type=f32) * score_scale).astype(
        dq_ref.dtype
    )
    head_k = (lax.dot_general(grad_score, q, first, preferred_element_type=f32) * score_scale)
    head_v = lax.dot_general(prob_half, g, first, preferred_element_type=f32)
    rows = q.shape[0]
    for slot, out_ref in enumerate(dkv_refs):
        out_ref[0] = head_k[slot * rows : (slot + 1) * rows].astype(out_ref.dtype)
        out_ref[1] = head_v[slot * rows : (slot + 1) * rows].astype(out_ref.dtype)


def chunk_call(mask, queries, grad_out, kv_slots, chunk, chunk_heads):
    rows = queries.shape[0]
    ctx_cols = mask.shape[1]
    head0 = chunk * chunk_heads
    row_spec = pl.BlockSpec((rows, DH), lambda h: (0, head0 + h))
    kv_spec = pl.BlockSpec((2, rows, DH), lambda h: (0, 0, h))
    kv_shape = jax.ShapeDtypeStruct((2, rows, chunk_heads * DH), jnp.bfloat16)
    return pl.pallas_call(
        head_kernel,
        grid=(chunk_heads,),
        in_specs=[pl.BlockSpec((rows, ctx_cols), lambda h: (0, 0)), row_spec, row_spec]
        + [kv_spec] * SLOTS,
        out_specs=[pl.BlockSpec((rows, DH), lambda h: (0, h))] + [kv_spec] * SLOTS,
        out_shape=[jax.ShapeDtypeStruct((rows, chunk_heads * DH), jnp.bfloat16)]
        + [kv_shape] * SLOTS,
        compiler_params=pltpu.CompilerParams(vmem_limit_bytes=48 * 1024 * 1024),
    )(mask, queries, grad_out, *kv_slots)


def body(queries, keys, values, grad_out, view_mask, tile_mask):
    tok_rows, feature_width = queries.shape
    dev_blocks = tok_rows // BLK
    camera_span = lax.axis_size("seq") // CAMS
    shifts = (camera_span, 1, 0, -1, -camera_span)
    blocks = block_allowed(view_mask, tile_mask, dev_blocks)
    mask = expand_blocks(blocks).astype(jnp.int32)
    head_count = feature_width // DH
    chunk_heads = head_count // CHUNKS
    chunk_width = chunk_heads * DH
    stacked = jnp.stack([keys, values]).reshape(2, tok_rows, CHUNKS, chunk_width)
    stacked = jnp.transpose(stacked, (2, 0, 1, 3))
    out_q, out_kv = [], []
    for chunk in range(CHUNKS):
        pair = stacked[chunk]
        kv_slots = [pair if shift == 0 else from_behind(pair, "seq", shift) for shift in shifts]
        head_q, *dkv = chunk_call(mask, queries, grad_out, kv_slots, chunk, chunk_heads)
        summed = dkv[2].astype(jnp.float32)
        for slot_index in (0, 1, 3, 4):
            back = from_behind(dkv[slot_index], "seq", -shifts[slot_index])
            summed = summed + back.astype(jnp.float32)
        out_q.append(head_q)
        out_kv.append(summed.astype(jnp.bfloat16))
    grad_kv = jnp.concatenate(out_kv, axis=2)
    return (jnp.concatenate(out_q, axis=1), grad_kv[0], grad_kv[1])


def solution(mesh):
    placed = (
        P(("group", "seq"), None),
        P(("group", "seq"), None),
        P(("group", "seq"), None),
        P(("group", "seq"), None),
        P(("group", "seq"), None),
        P(("group", "seq"), None),
    )
    return jax.shard_map(
        body,
        mesh=mesh,
        in_specs=placed,
        out_specs=(P(("group", "seq"), None), P(("group", "seq"), None), P(("group", "seq"), None)),
        check_vma=False,
    )
```

```python
import jax
import jax.numpy as jnp
from jax import lax
from jax.experimental import pallas as pl
from jax.experimental.pallas import tpu as pltpu
from jax.sharding import PartitionSpec as P

DH = 128
BLK = 128
CAMS = 4
CHUNKS = 2
SLOTS = 5
OWN = 2
ROWS = 8


LAST = (((1,), (1,)), ((), ()))
FIRST = (((0,), (0,)), ((), ()))


def from_behind(block, axis, distance):
    devices = range(lax.axis_size(axis))
    route = [((i - distance) % len(devices), i) for i in devices]
    return lax.ppermute(block, axis, route)


def block_allowed(view_rows, tile_rows, dev_blocks):
    joined = jnp.concatenate(
        [view_rows[:, :dev_blocks], tile_rows, view_rows[:, dev_blocks:]], axis=1
    )
    block_count = joined.shape[0]
    own_column = (
        2 * dev_blocks
        + lax.broadcasted_iota(jnp.int32, (block_count, 5 * dev_blocks), 0) % dev_blocks
    )
    column = lax.broadcasted_iota(jnp.int32, (block_count, 5 * dev_blocks), 1)
    return jnp.where(column == own_column, 1, joined)


def transposed_scores(kv_ref, qg_ref, mask_ref):
    score_scale = DH ** (-0.5)
    raw = lax.dot_general(kv_ref[0], qg_ref[0], LAST, preferred_element_type=jnp.float32)
    return jnp.where(mask_ref[...] > 0, raw * score_scale, -jnp.inf)


def stats_kernel(kv_ref, *refs):
    qg_refs = refs[:SLOTS]
    mask_refs = refs[SLOTS : 2 * SLOTS]
    stats_ref = refs[2 * SLOTS]
    f32 = jnp.float32
    for slot in range(SLOTS):
        scores = transposed_scores(kv_ref, qg_refs[slot], mask_refs[slot])
        top = jnp.max(scores, axis=0, keepdims=True)
        safe_top = jnp.where(top == -jnp.inf, 0.0, top)
        weights = jnp.exp(scores - safe_top)
        total = jnp.sum(weights, axis=0, keepdims=True)
        grad_prob = lax.dot_general(kv_ref[1], qg_refs[slot][1], LAST, preferred_element_type=f32)
        weighted = jnp.sum(weights * grad_prob, axis=0, keepdims=True)
        pad = jnp.zeros((ROWS - 3, top.shape[1]), f32)
        stats_ref[slot, 0] = jnp.concatenate([top, total, weighted, pad], axis=0)


def grad_kernel(kv_ref, *refs):
    qg_refs = refs[:SLOTS]
    mask_refs = refs[SLOTS : 2 * SLOTS]
    ld_refs = refs[2 * SLOTS : 3 * SLOTS]
    dkv_ref = refs[3 * SLOTS]
    dq_refs = refs[3 * SLOTS + 1 :]
    f32 = jnp.float32
    bf16 = jnp.bfloat16
    score_scale = DH ** (-0.5)
    acc_k = jnp.zeros(dkv_ref.shape[1:], f32)
    acc_v = jnp.zeros(dkv_ref.shape[1:], f32)
    for slot in range(SLOTS):
        scores = transposed_scores(kv_ref, qg_refs[slot], mask_refs[slot])
        rows = ld_refs[slot][0]
        log_total = rows[0:1, :]
        row_delta = rows[1:2, :]
        prob_full = jnp.exp(scores - log_total)
        prob_half = prob_full.astype(bf16)
        grad_prob = lax.dot_general(kv_ref[1], qg_refs[slot][1], LAST, preferred_element_type=f32)
        grad_score = (prob_full * (grad_prob - row_delta)).astype(bf16)
        part_k = jnp.dot(grad_score, qg_refs[slot][0], preferred_element_type=f32) * score_scale
        part_v = jnp.dot(prob_half, qg_refs[slot][1], preferred_element_type=f32)
        acc_k = acc_k + part_k.astype(bf16).astype(f32)
        acc_v = acc_v + part_v.astype(bf16).astype(f32)
        part_q = lax.dot_general(grad_score, kv_ref[0], FIRST, preferred_element_type=f32)
        dq_refs[slot][...] = (part_q * score_scale).astype(dq_refs[slot].dtype)
    dkv_ref[0] = acc_k.astype(bf16)
    dkv_ref[1] = acc_v.astype(bf16)


def specs(rows, chunk, chunk_heads):
    pair = pl.BlockSpec((2, rows, DH), lambda h: (0, 0, h))
    mask = pl.BlockSpec((rows, rows), lambda h: (0, 0))
    return pair, mask


def stats_call(kv, qg_slots, masks, chunk_heads):
    rows = kv.shape[1]
    pair, mask = specs(rows, 0, chunk_heads)
    return pl.pallas_call(
        stats_kernel,
        grid=(chunk_heads,),
        in_specs=[pair] + [pair] * SLOTS + [mask] * SLOTS,
        out_specs=pl.BlockSpec((SLOTS, 1, ROWS, rows), lambda h: (0, h, 0, 0)),
        out_shape=jax.ShapeDtypeStruct((SLOTS, chunk_heads, ROWS, rows), jnp.float32),
        compiler_params=pltpu.CompilerParams(vmem_limit_bytes=48 * 1024 * 1024),
    )(kv, *qg_slots, *masks)


def grad_call(kv, qg_slots, masks, ld_slots, chunk_heads):
    rows = kv.shape[1]
    pair, mask = specs(rows, 0, chunk_heads)
    ld_spec = pl.BlockSpec((1, ROWS, rows), lambda h: (h, 0, 0))
    row_spec = pl.BlockSpec((rows, DH), lambda h: (0, h))
    width = chunk_heads * DH
    dq_shapes = [
        jax.ShapeDtypeStruct((rows, width), jnp.float32 if slot == OWN else jnp.bfloat16)
        for slot in range(SLOTS)
    ]
    return pl.pallas_call(
        grad_kernel,
        grid=(chunk_heads,),
        in_specs=[pair] + [pair] * SLOTS + [mask] * SLOTS + [ld_spec] * SLOTS,
        out_specs=[pair] + [row_spec] * SLOTS,
        out_shape=[jax.ShapeDtypeStruct((2, rows, width), jnp.bfloat16)] + dq_shapes,
        compiler_params=pltpu.CompilerParams(vmem_limit_bytes=48 * 1024 * 1024),
    )(kv, *qg_slots, *masks, *ld_slots)


def body(queries, keys, values, grad_out, view_mask, tile_mask):
    tok_rows, feature_width = queries.shape
    dev_blocks = tok_rows // BLK
    seq_size = lax.axis_size("seq")
    camera_span = seq_size // CAMS
    shifts = (camera_span, 1, 0, -1, -camera_span)
    blocks = block_allowed(view_mask, tile_mask, dev_blocks)
    all_blocks = lax.all_gather(blocks, "seq")
    me = lax.axis_index("seq")
    masks = []
    for slot, shift in enumerate(shifts):
        owner_blocks = lax.dynamic_index_in_dim(all_blocks, (me + shift) % seq_size, 0, False)
        cut = owner_blocks[:, slot * dev_blocks : (slot + 1) * dev_blocks]
        spread = jnp.broadcast_to(cut.T[:, None, :, None], (dev_blocks, BLK, dev_blocks, BLK))
        masks.append(spread.reshape(tok_rows, tok_rows))
    head_count = feature_width // DH
    chunk_heads = head_count // CHUNKS
    chunk_width = chunk_heads * DH

    def by_chunk(first, second):
        stacked = jnp.stack([first, second]).reshape(2, tok_rows, CHUNKS, chunk_width)
        return jnp.transpose(stacked, (2, 0, 1, 3))

    kv_chunks = by_chunk(keys, values)
    qg_chunks = by_chunk(queries, grad_out)
    out_q, out_kv = [], []
    for chunk in range(CHUNKS):
        kv = kv_chunks[chunk]
        qg = qg_chunks[chunk]
        qg_slots = [qg if shift == 0 else from_behind(qg, "seq", -shift) for shift in shifts]
        stats = stats_call(kv, qg_slots, masks, chunk_heads)
        got = [
            stats[slot] if shift == 0 else from_behind(stats[slot], "seq", shift)
            for slot, shift in enumerate(shifts)
        ]
        got = jnp.stack(got)
        tops = got[:, :, 0]
        overall = jnp.max(tops, axis=0)
        scale = jnp.exp(tops - overall[None])
        log_total = overall + jnp.log(jnp.sum(got[:, :, 1] * scale, axis=0))
        row_delta = jnp.sum(got[:, :, 2] * jnp.exp(tops - log_total[None]), axis=0)
        pad = jnp.zeros((chunk_heads, ROWS - 2, tok_rows), jnp.float32)
        ld = jnp.concatenate([log_total[:, None], row_delta[:, None], pad], axis=1)
        ld_slots = [ld if shift == 0 else from_behind(ld, "seq", -shift) for shift in shifts]
        dkv, *dq_parts = grad_call(kv, qg_slots, masks, ld_slots, chunk_heads)
        summed = dq_parts[OWN]
        for slot, shift in enumerate(shifts):
            if shift != 0:
                summed = summed + from_behind(dq_parts[slot], "seq", shift).astype(jnp.float32)
        out_q.append(summed.astype(jnp.bfloat16))
        out_kv.append(dkv)
    grad_kv = jnp.concatenate(out_kv, axis=2)
    return (jnp.concatenate(out_q, axis=1), grad_kv[0], grad_kv[1])


def solution(mesh):
    placed = (
        P(("group", "seq"), None),
        P(("group", "seq"), None),
        P(("group", "seq"), None),
        P(("group", "seq"), None),
        P(("group", "seq"), None),
        P(("group", "seq"), None),
    )
    return jax.shard_map(
        body,
        mesh=mesh,
        in_specs=placed,
        out_specs=(P(("group", "seq"), None), P(("group", "seq"), None), P(("group", "seq"), None)),
        check_vma=False,
    )
```

```python
import jax
import jax.numpy as jnp
from jax import lax
from jax.experimental import pallas as pl
from jax.experimental.pallas import tpu as pltpu
from jax.sharding import PartitionSpec as P

DH = 128
BLK = 128
CAMS = 4
CHUNKS = 2
SLOTS = 5
OWN = 2
ROWS = 8


LAST = (((1,), (1,)), ((), ()))
FIRST = (((0,), (0,)), ((), ()))


def from_behind(block, axis, distance):
    devices = range(lax.axis_size(axis))
    route = [((i - distance) % len(devices), i) for i in devices]
    return lax.ppermute(block, axis, route)


def block_allowed(view_rows, tile_rows, dev_blocks):
    joined = jnp.concatenate(
        [view_rows[:, :dev_blocks], tile_rows, view_rows[:, dev_blocks:]], axis=1
    )
    block_count = joined.shape[0]
    own_column = (
        2 * dev_blocks
        + lax.broadcasted_iota(jnp.int32, (block_count, 5 * dev_blocks), 0) % dev_blocks
    )
    column = lax.broadcasted_iota(jnp.int32, (block_count, 5 * dev_blocks), 1)
    return jnp.where(column == own_column, 1, joined)


def transposed_scores(kv_ref, qg_ref):
    score_scale = DH ** (-0.5)
    raw = lax.dot_general(kv_ref[0], qg_ref[0], LAST, preferred_element_type=jnp.float32)
    return raw * score_scale


def stats_kernel(kv_ref, *refs):
    qg_refs = refs[:SLOTS]
    stats_ref = refs[SLOTS]
    f32 = jnp.float32
    for slot in range(SLOTS):
        scores = transposed_scores(kv_ref, qg_refs[slot])
        grad_prob = lax.dot_general(kv_ref[1], qg_refs[slot][1], LAST, preferred_element_type=f32)
        rows = []
        for low in range(0, scores.shape[0], BLK):
            part = scores[low : low + BLK]
            top = jnp.max(part, axis=0, keepdims=True)
            weights = jnp.exp(part - top)
            total = jnp.sum(weights, axis=0, keepdims=True)
            weighted = jnp.sum(weights * grad_prob[low : low + BLK], axis=0, keepdims=True)
            rows += [top, total, weighted]
        pad = jnp.zeros((ROWS - len(rows), scores.shape[1]), f32)
        stats_ref[slot, 0] = jnp.concatenate(rows + [pad], axis=0)


def grad_kernel(kv_ref, *refs):
    qg_refs = refs[:SLOTS]
    ld_refs = refs[SLOTS : 2 * SLOTS]
    dkv_ref = refs[2 * SLOTS]
    dq_refs = refs[2 * SLOTS + 1 :]
    f32 = jnp.float32
    bf16 = jnp.bfloat16
    score_scale = DH ** (-0.5)
    acc_k = jnp.zeros(dkv_ref.shape[1:], f32)
    acc_v = jnp.zeros(dkv_ref.shape[1:], f32)
    for slot in range(SLOTS):
        scores = transposed_scores(kv_ref, qg_refs[slot])
        rows = ld_refs[slot][0]
        key_blocks = scores.shape[0] // BLK
        log_total = jnp.concatenate(
            [jnp.broadcast_to(rows[kb : kb + 1, :], (BLK, scores.shape[1])) for kb in range(key_blocks)],
            axis=0,
        )
        row_delta = rows[key_blocks : key_blocks + 1, :]
        prob_full = jnp.exp(scores - log_total)
        prob_half = prob_full.astype(bf16)
        grad_prob = lax.dot_general(kv_ref[1], qg_refs[slot][1], LAST, preferred_element_type=f32)
        grad_score = (prob_full * (grad_prob - row_delta)).astype(bf16)
        part_k = jnp.dot(grad_score, qg_refs[slot][0], preferred_element_type=f32) * score_scale
        part_v = jnp.dot(prob_half, qg_refs[slot][1], preferred_element_type=f32)
        acc_k = acc_k + part_k.astype(bf16).astype(f32)
        acc_v = acc_v + part_v.astype(bf16).astype(f32)
        part_q = lax.dot_general(grad_score, kv_ref[0], FIRST, preferred_element_type=f32)
        dq_refs[slot][...] = (part_q * score_scale).astype(dq_refs[slot].dtype)
    dkv_ref[0] = acc_k.astype(bf16)
    dkv_ref[1] = acc_v.astype(bf16)


def stats_call(kv, qg_slots, chunk_heads):
    rows = kv.shape[1]
    pair = pl.BlockSpec((2, rows, DH), lambda h: (0, 0, h))
    return pl.pallas_call(
        stats_kernel,
        grid=(chunk_heads,),
        in_specs=[pair] + [pair] * SLOTS,
        out_specs=pl.BlockSpec((SLOTS, 1, ROWS, rows), lambda h: (0, h, 0, 0)),
        out_shape=jax.ShapeDtypeStruct((SLOTS, chunk_heads, ROWS, rows), jnp.float32),
        compiler_params=pltpu.CompilerParams(vmem_limit_bytes=48 * 1024 * 1024),
    )(kv, *qg_slots)


def grad_call(kv, qg_slots, ld_slots, chunk_heads):
    rows = kv.shape[1]
    pair = pl.BlockSpec((2, rows, DH), lambda h: (0, 0, h))
    ld_spec = pl.BlockSpec((1, ROWS, rows), lambda h: (h, 0, 0))
    row_spec = pl.BlockSpec((rows, DH), lambda h: (0, h))
    width = chunk_heads * DH
    dq_shapes = [
        jax.ShapeDtypeStruct((rows, width), jnp.float32 if slot == OWN else jnp.bfloat16)
        for slot in range(SLOTS)
    ]
    return pl.pallas_call(
        grad_kernel,
        grid=(chunk_heads,),
        in_specs=[pair] + [pair] * SLOTS + [ld_spec] * SLOTS,
        out_specs=[pair] + [row_spec] * SLOTS,
        out_shape=[jax.ShapeDtypeStruct((2, rows, width), jnp.bfloat16)] + dq_shapes,
        compiler_params=pltpu.CompilerParams(vmem_limit_bytes=48 * 1024 * 1024),
    )(kv, *qg_slots, *ld_slots)


def body(queries, keys, values, grad_out, view_mask, tile_mask):
    tok_rows, feature_width = queries.shape
    dev_blocks = tok_rows // BLK
    seq_size = lax.axis_size("seq")
    camera_span = seq_size // CAMS
    shifts = (camera_span, 1, 0, -1, -camera_span)
    blocks = block_allowed(view_mask, tile_mask, dev_blocks)
    allowed = jnp.repeat(blocks.T, BLK, axis=1).reshape(SLOTS, dev_blocks, 1, tok_rows) > 0
    head_count = feature_width // DH
    chunk_heads = head_count // CHUNKS
    chunk_width = chunk_heads * DH

    def by_chunk(first, second):
        stacked = jnp.stack([first, second]).reshape(2, tok_rows, CHUNKS, chunk_width)
        return jnp.transpose(stacked, (2, 0, 1, 3))

    kv_chunks = by_chunk(keys, values)
    qg_chunks = by_chunk(queries, grad_out)
    out_q, out_kv = [], []
    for chunk in range(CHUNKS):
        kv = kv_chunks[chunk]
        qg = qg_chunks[chunk]
        qg_slots = [qg if shift == 0 else from_behind(qg, "seq", -shift) for shift in shifts]
        stats = stats_call(kv, qg_slots, chunk_heads)
        got = [
            stats[slot] if shift == 0 else from_behind(stats[slot], "seq", shift)
            for slot, shift in enumerate(shifts)
        ]
        got = jnp.stack(got)[:, :, : 3 * dev_blocks].reshape(
            SLOTS, chunk_heads, dev_blocks, 3, tok_rows
        )
        got = jnp.transpose(got, (0, 2, 3, 1, 4))
        tops = jnp.where(allowed, got[:, :, 0], -jnp.inf)
        totals = jnp.where(allowed, got[:, :, 1], 0.0)
        weighted = jnp.where(allowed, got[:, :, 2], 0.0)
        overall = jnp.max(tops, axis=(0, 1))
        log_total = overall + jnp.log(jnp.sum(totals * jnp.exp(tops - overall), axis=(0, 1)))
        row_delta = jnp.sum(weighted * jnp.exp(tops - log_total), axis=(0, 1))
        pad = jnp.zeros((chunk_heads, ROWS - dev_blocks - 1, tok_rows), jnp.float32)
        ld_slots = []
        for slot, shift in enumerate(shifts):
            per_block = jnp.where(allowed[slot], log_total[None], jnp.inf)
            ld = jnp.concatenate(
                [jnp.transpose(per_block, (1, 0, 2)), row_delta[:, None], pad], axis=1
            )
            ld_slots.append(ld if shift == 0 else from_behind(ld, "seq", -shift))
        dkv, *dq_parts = grad_call(kv, qg_slots, ld_slots, chunk_heads)
        summed = dq_parts[OWN]
        for slot, shift in enumerate(shifts):
            if shift != 0:
                summed = summed + from_behind(dq_parts[slot], "seq", shift).astype(jnp.float32)
        out_q.append(summed.astype(jnp.bfloat16))
        out_kv.append(dkv)
    grad_kv = jnp.concatenate(out_kv, axis=2)
    return (jnp.concatenate(out_q, axis=1), grad_kv[0], grad_kv[1])


def solution(mesh):
    placed = (
        P(("group", "seq"), None),
        P(("group", "seq"), None),
        P(("group", "seq"), None),
        P(("group", "seq"), None),
        P(("group", "seq"), None),
        P(("group", "seq"), None),
    )
    return jax.shard_map(
        body,
        mesh=mesh,
        in_specs=placed,
        out_specs=(P(("group", "seq"), None), P(("group", "seq"), None), P(("group", "seq"), None)),
        check_vma=False,
    )
```

```python
import jax
import jax.numpy as jnp
from jax import lax
from jax.experimental import pallas as pl
from jax.experimental.pallas import tpu as pltpu
from jax.sharding import PartitionSpec as P

DH = 128
BLK = 128
CAMS = 4
CHUNKS = 4
SLOTS = 5
OWN = 2
ROWS = 8


LAST = (((1,), (1,)), ((), ()))
FIRST = (((0,), (0,)), ((), ()))


def from_behind(block, axis, distance):
    devices = range(lax.axis_size(axis))
    route = [((i - distance) % len(devices), i) for i in devices]
    return lax.ppermute(block, axis, route)


def block_allowed(view_rows, tile_rows, dev_blocks):
    joined = jnp.concatenate(
        [view_rows[:, :dev_blocks], tile_rows, view_rows[:, dev_blocks:]], axis=1
    )
    block_count = joined.shape[0]
    own_column = (
        2 * dev_blocks
        + lax.broadcasted_iota(jnp.int32, (block_count, 5 * dev_blocks), 0) % dev_blocks
    )
    column = lax.broadcasted_iota(jnp.int32, (block_count, 5 * dev_blocks), 1)
    return jnp.where(column == own_column, 1, joined)


def transposed_scores(kv_ref, qg_ref):
    score_scale = DH ** (-0.5)
    raw = lax.dot_general(kv_ref[0], qg_ref[0], LAST, preferred_element_type=jnp.float32)
    return raw * score_scale


def stats_kernel(kv_ref, *refs):
    qg_refs = refs[:SLOTS]
    stats_ref = refs[SLOTS]
    f32 = jnp.float32
    for slot in range(SLOTS):
        scores = transposed_scores(kv_ref, qg_refs[slot])
        grad_prob = lax.dot_general(kv_ref[1], qg_refs[slot][1], LAST, preferred_element_type=f32)
        rows = []
        for low in range(0, scores.shape[0], BLK):
            part = scores[low : low + BLK]
            top = jnp.max(part, axis=0, keepdims=True)
            weights = jnp.exp(part - top)
            total = jnp.sum(weights, axis=0, keepdims=True)
            weighted = jnp.sum(weights * grad_prob[low : low + BLK], axis=0, keepdims=True)
            rows += [top, total, weighted]
        pad = jnp.zeros((ROWS - len(rows), scores.shape[1]), f32)
        stats_ref[slot, 0] = jnp.concatenate(rows + [pad], axis=0)


def grad_kernel(kv_ref, *refs):
    qg_refs = refs[:SLOTS]
    ld_refs = refs[SLOTS : 2 * SLOTS]
    dkv_ref = refs[2 * SLOTS]
    dq_refs = refs[2 * SLOTS + 1 :]
    f32 = jnp.float32
    bf16 = jnp.bfloat16
    score_scale = DH ** (-0.5)
    acc_k = jnp.zeros(dkv_ref.shape[1:], f32)
    acc_v = jnp.zeros(dkv_ref.shape[1:], f32)
    for slot in range(SLOTS):
        scores = transposed_scores(kv_ref, qg_refs[slot])
        rows = ld_refs[slot][0]
        key_blocks = scores.shape[0] // BLK
        log_total = jnp.concatenate(
            [jnp.broadcast_to(rows[kb : kb + 1, :], (BLK, scores.shape[1])) for kb in range(key_blocks)],
            axis=0,
        )
        row_delta = rows[key_blocks : key_blocks + 1, :]
        prob_full = jnp.exp(scores - log_total)
        prob_half = prob_full.astype(bf16)
        grad_prob = lax.dot_general(kv_ref[1], qg_refs[slot][1], LAST, preferred_element_type=f32)
        grad_score = (prob_full * (grad_prob - row_delta)).astype(bf16)
        part_k = jnp.dot(grad_score, qg_refs[slot][0], preferred_element_type=f32) * score_scale
        part_v = jnp.dot(prob_half, qg_refs[slot][1], preferred_element_type=f32)
        acc_k = acc_k + part_k.astype(bf16).astype(f32)
        acc_v = acc_v + part_v.astype(bf16).astype(f32)
        part_q = lax.dot_general(grad_score, kv_ref[0], FIRST, preferred_element_type=f32)
        dq_refs[slot][...] = (part_q * score_scale).astype(dq_refs[slot].dtype)
    dkv_ref[0] = acc_k.astype(bf16)
    dkv_ref[1] = acc_v.astype(bf16)


def stats_call(kv, qg_slots, chunk_heads):
    rows = kv.shape[1]
    pair = pl.BlockSpec((2, rows, DH), lambda h: (0, 0, h))
    return pl.pallas_call(
        stats_kernel,
        grid=(chunk_heads,),
        in_specs=[pair] + [pair] * SLOTS,
        out_specs=pl.BlockSpec((SLOTS, 1, ROWS, rows), lambda h: (0, h, 0, 0)),
        out_shape=jax.ShapeDtypeStruct((SLOTS, chunk_heads, ROWS, rows), jnp.float32),
        compiler_params=pltpu.CompilerParams(vmem_limit_bytes=48 * 1024 * 1024),
    )(kv, *qg_slots)


def grad_call(kv, qg_slots, ld_slots, chunk_heads):
    rows = kv.shape[1]
    pair = pl.BlockSpec((2, rows, DH), lambda h: (0, 0, h))
    ld_spec = pl.BlockSpec((1, ROWS, rows), lambda h: (h, 0, 0))
    row_spec = pl.BlockSpec((rows, DH), lambda h: (0, h))
    width = chunk_heads * DH
    dq_shapes = [
        jax.ShapeDtypeStruct((rows, width), jnp.float32 if slot == OWN else jnp.bfloat16)
        for slot in range(SLOTS)
    ]
    return pl.pallas_call(
        grad_kernel,
        grid=(chunk_heads,),
        in_specs=[pair] + [pair] * SLOTS + [ld_spec] * SLOTS,
        out_specs=[pair] + [row_spec] * SLOTS,
        out_shape=[jax.ShapeDtypeStruct((2, rows, width), jnp.bfloat16)] + dq_shapes,
        compiler_params=pltpu.CompilerParams(vmem_limit_bytes=48 * 1024 * 1024),
    )(kv, *qg_slots, *ld_slots)


def body(queries, keys, values, grad_out, view_mask, tile_mask):
    tok_rows, feature_width = queries.shape
    dev_blocks = tok_rows // BLK
    seq_size = lax.axis_size("seq")
    camera_span = seq_size // CAMS
    shifts = (camera_span, 1, 0, -1, -camera_span)
    blocks = block_allowed(view_mask, tile_mask, dev_blocks)
    allowed = jnp.repeat(blocks.T, BLK, axis=1).reshape(SLOTS, dev_blocks, 1, tok_rows) > 0
    head_count = feature_width // DH
    chunk_heads = head_count // CHUNKS
    chunk_width = chunk_heads * DH

    def by_chunk(first, second):
        stacked = jnp.stack([first, second]).reshape(2, tok_rows, CHUNKS, chunk_width)
        return jnp.transpose(stacked, (2, 0, 1, 3))

    kv_chunks = by_chunk(keys, values)
    qg_chunks = by_chunk(queries, grad_out)
    out_q, out_kv = [], []
    arrived = ()
    for chunk in range(CHUNKS):
        kv = kv_chunks[chunk]
        qg, _ = lax.optimization_barrier((qg_chunks[chunk], arrived))
        qg_slots = [qg if shift == 0 else from_behind(qg, "seq", -shift) for shift in shifts]
        arrived = tuple(qg_slots[slot] for slot, shift in enumerate(shifts) if shift != 0)
        stats = stats_call(kv, qg_slots, chunk_heads)
        got = [
            stats[slot] if shift == 0 else from_behind(stats[slot], "seq", shift)
            for slot, shift in enumerate(shifts)
        ]
        got = jnp.stack(got)[:, :, : 3 * dev_blocks].reshape(
            SLOTS, chunk_heads, dev_blocks, 3, tok_rows
        )
        got = jnp.transpose(got, (0, 2, 3, 1, 4))
        tops = jnp.where(allowed, got[:, :, 0], -jnp.inf)
        totals = jnp.where(allowed, got[:, :, 1], 0.0)
        weighted = jnp.where(allowed, got[:, :, 2], 0.0)
        overall = jnp.max(tops, axis=(0, 1))
        log_total = overall + jnp.log(jnp.sum(totals * jnp.exp(tops - overall), axis=(0, 1)))
        row_delta = jnp.sum(weighted * jnp.exp(tops - log_total), axis=(0, 1))
        pad = jnp.zeros((chunk_heads, ROWS - dev_blocks - 1, tok_rows), jnp.float32)
        ld_slots = []
        for slot, shift in enumerate(shifts):
            per_block = jnp.where(allowed[slot], log_total[None], jnp.inf)
            ld = jnp.concatenate(
                [jnp.transpose(per_block, (1, 0, 2)), row_delta[:, None], pad], axis=1
            )
            ld_slots.append(ld if shift == 0 else from_behind(ld, "seq", -shift))
        dkv, *dq_parts = grad_call(kv, qg_slots, ld_slots, chunk_heads)
        summed = dq_parts[OWN]
        for slot, shift in enumerate(shifts):
            if shift != 0:
                summed = summed + from_behind(dq_parts[slot], "seq", shift).astype(jnp.float32)
        out_q.append(summed.astype(jnp.bfloat16))
        out_kv.append(dkv)
    grad_kv = jnp.concatenate(out_kv, axis=2)
    return (jnp.concatenate(out_q, axis=1), grad_kv[0], grad_kv[1])


def solution(mesh):
    placed = (
        P(("group", "seq"), None),
        P(("group", "seq"), None),
        P(("group", "seq"), None),
        P(("group", "seq"), None),
        P(("group", "seq"), None),
        P(("group", "seq"), None),
    )
    return jax.shard_map(
        body,
        mesh=mesh,
        in_specs=placed,
        out_specs=(P(("group", "seq"), None), P(("group", "seq"), None), P(("group", "seq"), None)),
        check_vma=False,
    )
```

```python
import jax
import jax.numpy as jnp
from jax import lax
from jax.experimental import pallas as pl
from jax.experimental.pallas import tpu as pltpu
from jax.sharding import PartitionSpec as P

DH = 128
BLK = 128
CAMS = 4
CHUNKS = 2
SLOTS = 5
OWN = 2
ROWS = 8


LAST = (((1,), (1,)), ((), ()))
FIRST = (((0,), (0,)), ((), ()))


def from_behind(block, axis, distance):
    devices = range(lax.axis_size(axis))
    route = [((i - distance) % len(devices), i) for i in devices]
    return lax.ppermute(block, axis, route)


def block_allowed(view_rows, tile_rows, dev_blocks):
    joined = jnp.concatenate(
        [view_rows[:, :dev_blocks], tile_rows, view_rows[:, dev_blocks:]], axis=1
    )
    block_count = joined.shape[0]
    own_column = (
        2 * dev_blocks
        + lax.broadcasted_iota(jnp.int32, (block_count, 5 * dev_blocks), 0) % dev_blocks
    )
    column = lax.broadcasted_iota(jnp.int32, (block_count, 5 * dev_blocks), 1)
    return jnp.where(column == own_column, 1, joined)


def transposed_scores(kv_ref, qg_ref):
    score_scale = DH ** (-0.5)
    raw = lax.dot_general(kv_ref[0], qg_ref[0], LAST, preferred_element_type=jnp.float32)
    return raw * score_scale


def stats_kernel(kv_ref, *refs):
    qg_refs = refs[:SLOTS]
    stats_ref = refs[SLOTS]
    f32 = jnp.float32
    for slot in range(SLOTS):
        scores = transposed_scores(kv_ref, qg_refs[slot])
        grad_prob = lax.dot_general(kv_ref[1], qg_refs[slot][1], LAST, preferred_element_type=f32)
        rows = []
        for low in range(0, scores.shape[0], BLK):
            part = scores[low : low + BLK]
            top = jnp.max(part, axis=0, keepdims=True)
            weights = jnp.exp(part - top)
            total = jnp.sum(weights, axis=0, keepdims=True)
            weighted = jnp.sum(weights * grad_prob[low : low + BLK], axis=0, keepdims=True)
            rows += [top, total, weighted]
        pad = jnp.zeros((ROWS - len(rows), scores.shape[1]), f32)
        stats_ref[slot, 0] = jnp.concatenate(rows + [pad], axis=0)


def grad_kernel(kv_ref, *refs):
    qg_refs = refs[:SLOTS]
    ld_refs = refs[SLOTS : 2 * SLOTS]
    dkv_ref = refs[2 * SLOTS]
    dq_refs = refs[2 * SLOTS + 1 :]
    f32 = jnp.float32
    bf16 = jnp.bfloat16
    score_scale = DH ** (-0.5)
    acc_k = jnp.zeros(dkv_ref.shape[1:], f32)
    acc_v = jnp.zeros(dkv_ref.shape[1:], f32)
    for slot in range(SLOTS):
        scores = transposed_scores(kv_ref, qg_refs[slot])
        rows = ld_refs[slot][0]
        key_blocks = scores.shape[0] // BLK
        log_total = jnp.concatenate(
            [jnp.broadcast_to(rows[kb : kb + 1, :], (BLK, scores.shape[1])) for kb in range(key_blocks)],
            axis=0,
        )
        row_delta = rows[key_blocks : key_blocks + 1, :]
        prob_full = jnp.exp(scores - log_total)
        prob_half = prob_full.astype(bf16)
        grad_prob = lax.dot_general(kv_ref[1], qg_refs[slot][1], LAST, preferred_element_type=f32)
        grad_score = (prob_full * (grad_prob - row_delta)).astype(bf16)
        part_k = jnp.dot(grad_score, qg_refs[slot][0], preferred_element_type=f32) * score_scale
        part_v = jnp.dot(prob_half, qg_refs[slot][1], preferred_element_type=f32)
        acc_k = acc_k + part_k.astype(bf16).astype(f32)
        acc_v = acc_v + part_v.astype(bf16).astype(f32)
        part_q = lax.dot_general(grad_score, kv_ref[0], FIRST, preferred_element_type=f32)
        dq_refs[slot][...] = (part_q * score_scale).astype(dq_refs[slot].dtype)
    dkv_ref[0] = acc_k.astype(bf16)
    dkv_ref[1] = acc_v.astype(bf16)


def stats_call(kv, qg_slots, chunk_heads):
    rows = kv.shape[1]
    pair = pl.BlockSpec((2, rows, DH), lambda h: (0, 0, h))
    return pl.pallas_call(
        stats_kernel,
        grid=(chunk_heads,),
        in_specs=[pair] + [pair] * SLOTS,
        out_specs=pl.BlockSpec((SLOTS, 1, ROWS, rows), lambda h: (0, h, 0, 0)),
        out_shape=jax.ShapeDtypeStruct((SLOTS, chunk_heads, ROWS, rows), jnp.float32),
        compiler_params=pltpu.CompilerParams(vmem_limit_bytes=48 * 1024 * 1024),
    )(kv, *qg_slots)


def grad_call(kv, qg_slots, ld_slots, chunk_heads):
    rows = kv.shape[1]
    pair = pl.BlockSpec((2, rows, DH), lambda h: (0, 0, h))
    ld_spec = pl.BlockSpec((1, ROWS, rows), lambda h: (h, 0, 0))
    row_spec = pl.BlockSpec((rows, DH), lambda h: (0, h))
    width = chunk_heads * DH
    dq_shapes = [
        jax.ShapeDtypeStruct((rows, width), jnp.float32 if slot == OWN else jnp.bfloat16)
        for slot in range(SLOTS)
    ]
    return pl.pallas_call(
        grad_kernel,
        grid=(chunk_heads,),
        in_specs=[pair] + [pair] * SLOTS + [ld_spec] * SLOTS,
        out_specs=[pair] + [row_spec] * SLOTS,
        out_shape=[jax.ShapeDtypeStruct((2, rows, width), jnp.bfloat16)] + dq_shapes,
        compiler_params=pltpu.CompilerParams(vmem_limit_bytes=48 * 1024 * 1024),
    )(kv, *qg_slots, *ld_slots)


def body(queries, keys, values, grad_out, view_mask, tile_mask):
    tok_rows, feature_width = queries.shape
    dev_blocks = tok_rows // BLK
    seq_size = lax.axis_size("seq")
    camera_span = seq_size // CAMS
    shifts = (camera_span, 1, 0, -1, -camera_span)
    blocks = block_allowed(view_mask, tile_mask, dev_blocks)
    allowed = jnp.repeat(blocks.T, BLK, axis=1).reshape(SLOTS, dev_blocks, 1, tok_rows) > 0
    head_count = feature_width // DH
    chunk_heads = head_count // CHUNKS
    chunk_width = chunk_heads * DH

    def by_chunk(first, second):
        stacked = jnp.stack([first, second]).reshape(2, tok_rows, CHUNKS, chunk_width)
        return jnp.transpose(stacked, (2, 0, 1, 3))

    kv_chunks = by_chunk(keys, values)
    qg_chunks = by_chunk(queries, grad_out)
    out_q, out_kv = [], []
    arrived = ()
    for chunk in range(CHUNKS):
        kv = kv_chunks[chunk]
        qg, _ = lax.optimization_barrier((qg_chunks[chunk], arrived))
        qg_slots = [qg if shift == 0 else from_behind(qg, "seq", -shift) for shift in shifts]
        arrived = tuple(qg_slots[slot] for slot, shift in enumerate(shifts) if shift != 0)
        stats = stats_call(kv, qg_slots, chunk_heads)
        got = [
            stats[slot] if shift == 0 else from_behind(stats[slot], "seq", shift)
            for slot, shift in enumerate(shifts)
        ]
        got = jnp.stack(got)[:, :, : 3 * dev_blocks].reshape(
            SLOTS, chunk_heads, dev_blocks, 3, tok_rows
        )
        got = jnp.transpose(got, (0, 2, 3, 1, 4))
        tops = jnp.where(allowed, got[:, :, 0], -jnp.inf)
        totals = jnp.where(allowed, got[:, :, 1], 0.0)
        weighted = jnp.where(allowed, got[:, :, 2], 0.0)
        overall = jnp.max(tops, axis=(0, 1))
        log_total = overall + jnp.log(jnp.sum(totals * jnp.exp(tops - overall), axis=(0, 1)))
        row_delta = jnp.sum(weighted * jnp.exp(tops - log_total), axis=(0, 1))
        pad = jnp.zeros((chunk_heads, ROWS - dev_blocks - 1, tok_rows), jnp.float32)
        ld_slots = []
        for slot, shift in enumerate(shifts):
            per_block = jnp.where(allowed[slot], log_total[None], jnp.inf)
            ld = jnp.concatenate(
                [jnp.transpose(per_block, (1, 0, 2)), row_delta[:, None], pad], axis=1
            )
            ld_slots.append(ld if shift == 0 else from_behind(ld, "seq", -shift))
        dkv, *dq_parts = grad_call(kv, qg_slots, ld_slots, chunk_heads)
        summed = dq_parts[OWN]
        for slot, shift in enumerate(shifts):
            if shift != 0:
                summed = summed + from_behind(dq_parts[slot], "seq", shift).astype(jnp.float32)
        out_q.append(summed.astype(jnp.bfloat16))
        out_kv.append(dkv)
    grad_kv = jnp.concatenate(out_kv, axis=2)
    return (jnp.concatenate(out_q, axis=1), grad_kv[0], grad_kv[1])


def solution(mesh):
    placed = (
        P(("group", "seq"), None),
        P(("group", "seq"), None),
        P(("group", "seq"), None),
        P(("group", "seq"), None),
        P(("group", "seq"), None),
        P(("group", "seq"), None),
    )
    return jax.shard_map(
        body,
        mesh=mesh,
        in_specs=placed,
        out_specs=(P(("group", "seq"), None), P(("group", "seq"), None), P(("group", "seq"), None)),
        check_vma=False,
    )
```

```python
import jax
import jax.numpy as jnp
from jax import lax
from jax.experimental import pallas as pl
from jax.experimental.pallas import tpu as pltpu
from jax.sharding import PartitionSpec as P

DH = 128
BLK = 128
CAMS = 4
CHUNKS = 2
SLOTS = 5
OWN = 2
ROWS = 8


LAST = (((1,), (1,)), ((), ()))
FIRST = (((0,), (0,)), ((), ()))


def from_behind(block, axis, distance):
    devices = range(lax.axis_size(axis))
    route = [((i - distance) % len(devices), i) for i in devices]
    return lax.ppermute(block, axis, route)


def block_allowed(view_rows, tile_rows, dev_blocks):
    joined = jnp.concatenate(
        [view_rows[:, :dev_blocks], tile_rows, view_rows[:, dev_blocks:]], axis=1
    )
    block_count = joined.shape[0]
    own_column = (
        2 * dev_blocks
        + lax.broadcasted_iota(jnp.int32, (block_count, 5 * dev_blocks), 0) % dev_blocks
    )
    column = lax.broadcasted_iota(jnp.int32, (block_count, 5 * dev_blocks), 1)
    return jnp.where(column == own_column, 1, joined)


def transposed_scores(kv_ref, qg_ref):
    score_scale = DH ** (-0.5)
    raw = lax.dot_general(kv_ref[0], qg_ref[0], LAST, preferred_element_type=jnp.float32)
    return raw * score_scale


def stats_kernel(kv_ref, *refs):
    qg_refs = refs[:SLOTS]
    stats_ref = refs[SLOTS]
    f32 = jnp.float32
    for slot in range(SLOTS):
        scores = transposed_scores(kv_ref, qg_refs[slot])
        grad_prob = lax.dot_general(kv_ref[1], qg_refs[slot][1], LAST, preferred_element_type=f32)
        rows = []
        for low in range(0, scores.shape[0], BLK):
            part = scores[low : low + BLK]
            top = jnp.max(part, axis=0, keepdims=True)
            weights = jnp.exp(part - top)
            total = jnp.sum(weights, axis=0, keepdims=True)
            weighted = jnp.sum(weights * grad_prob[low : low + BLK], axis=0, keepdims=True)
            rows += [top, total, weighted]
        pad = jnp.zeros((ROWS - len(rows), scores.shape[1]), f32)
        stats_ref[slot, 0] = jnp.concatenate(rows + [pad], axis=0)


def grad_kernel(kv_ref, *refs):
    qg_refs = refs[:SLOTS]
    ld_refs = refs[SLOTS : 2 * SLOTS]
    dkv_ref = refs[2 * SLOTS]
    dq_refs = refs[2 * SLOTS + 1 :]
    f32 = jnp.float32
    bf16 = jnp.bfloat16
    score_scale = DH ** (-0.5)
    acc_k = jnp.zeros(dkv_ref.shape[1:], f32)
    acc_v = jnp.zeros(dkv_ref.shape[1:], f32)
    for slot in range(SLOTS):
        scores = transposed_scores(kv_ref, qg_refs[slot])
        rows = ld_refs[slot][0]
        key_blocks = scores.shape[0] // BLK
        log_total = jnp.concatenate(
            [jnp.broadcast_to(rows[kb : kb + 1, :], (BLK, scores.shape[1])) for kb in range(key_blocks)],
            axis=0,
        )
        row_delta = rows[key_blocks : key_blocks + 1, :]
        prob_full = jnp.exp(scores - log_total)
        prob_half = prob_full.astype(bf16)
        grad_prob = lax.dot_general(kv_ref[1], qg_refs[slot][1], LAST, preferred_element_type=f32)
        grad_score = (prob_full * (grad_prob - row_delta)).astype(bf16)
        part_k = jnp.dot(grad_score, qg_refs[slot][0], preferred_element_type=f32) * score_scale
        part_v = jnp.dot(prob_half, qg_refs[slot][1], preferred_element_type=f32)
        acc_k = acc_k + part_k.astype(bf16).astype(f32)
        acc_v = acc_v + part_v.astype(bf16).astype(f32)
        part_q = lax.dot_general(grad_score, kv_ref[0], FIRST, preferred_element_type=f32)
        dq_refs[slot][...] = (part_q * score_scale).astype(dq_refs[slot].dtype)
    dkv_ref[0] = acc_k.astype(bf16)
    dkv_ref[1] = acc_v.astype(bf16)


def stats_call(kv, qg_slots, chunk_heads):
    rows = kv.shape[1]
    pair = pl.BlockSpec((2, rows, DH), lambda h: (0, 0, h))
    return pl.pallas_call(
        stats_kernel,
        grid=(chunk_heads,),
        in_specs=[pair] + [pair] * SLOTS,
        out_specs=pl.BlockSpec((SLOTS, 1, ROWS, rows), lambda h: (0, h, 0, 0)),
        out_shape=jax.ShapeDtypeStruct((SLOTS, chunk_heads, ROWS, rows), jnp.float32),
        compiler_params=pltpu.CompilerParams(vmem_limit_bytes=48 * 1024 * 1024),
    )(kv, *qg_slots)


def grad_call(kv, qg_slots, ld_slots, chunk, chunk_heads):
    rows = kv.shape[1]
    pair = pl.BlockSpec((2, rows, DH), lambda h: (0, 0, h))
    head0 = chunk * chunk_heads
    ld_spec = pl.BlockSpec((1, ROWS, rows), lambda h: (head0 + h, 0, 0))
    row_spec = pl.BlockSpec((rows, DH), lambda h: (0, h))
    width = chunk_heads * DH
    dq_shapes = [
        jax.ShapeDtypeStruct((rows, width), jnp.float32 if slot == OWN else jnp.bfloat16)
        for slot in range(SLOTS)
    ]
    return pl.pallas_call(
        grad_kernel,
        grid=(chunk_heads,),
        in_specs=[pair] + [pair] * SLOTS + [ld_spec] * SLOTS,
        out_specs=[pair] + [row_spec] * SLOTS,
        out_shape=[jax.ShapeDtypeStruct((2, rows, width), jnp.bfloat16)] + dq_shapes,
        compiler_params=pltpu.CompilerParams(vmem_limit_bytes=48 * 1024 * 1024),
    )(kv, *qg_slots, *ld_slots)


def body(queries, keys, values, grad_out, view_mask, tile_mask):
    tok_rows, feature_width = queries.shape
    dev_blocks = tok_rows // BLK
    seq_size = lax.axis_size("seq")
    camera_span = seq_size // CAMS
    shifts = (camera_span, 1, 0, -1, -camera_span)
    blocks = block_allowed(view_mask, tile_mask, dev_blocks)
    allowed = jnp.repeat(blocks.T, BLK, axis=1).reshape(SLOTS, dev_blocks, 1, tok_rows) > 0
    head_count = feature_width // DH
    chunk_heads = head_count // CHUNKS
    chunk_width = chunk_heads * DH

    def by_chunk(first, second):
        stacked = jnp.stack([first, second]).reshape(2, tok_rows, CHUNKS, chunk_width)
        return jnp.transpose(stacked, (2, 0, 1, 3))

    kv_chunks = by_chunk(keys, values)
    qg_chunks = by_chunk(queries, grad_out)
    qg_by_chunk, stats_by_chunk = [], []
    for chunk in range(CHUNKS):
        qg = qg_chunks[chunk]
        qg_slots = [qg if shift == 0 else from_behind(qg, "seq", -shift) for shift in shifts]
        qg_by_chunk.append(qg_slots)
        stats_by_chunk.append(stats_call(kv_chunks[chunk], qg_slots, chunk_heads))
    stats = jnp.concatenate(stats_by_chunk, axis=1)
    got = [
        stats[slot] if shift == 0 else from_behind(stats[slot], "seq", shift)
        for slot, shift in enumerate(shifts)
    ]
    got = jnp.stack(got)[:, :, : 3 * dev_blocks].reshape(
        SLOTS, head_count, dev_blocks, 3, tok_rows
    )
    got = jnp.transpose(got, (0, 2, 3, 1, 4))
    tops = jnp.where(allowed, got[:, :, 0], -jnp.inf)
    totals = jnp.where(allowed, got[:, :, 1], 0.0)
    weighted = jnp.where(allowed, got[:, :, 2], 0.0)
    overall = jnp.max(tops, axis=(0, 1))
    log_total = overall + jnp.log(jnp.sum(totals * jnp.exp(tops - overall), axis=(0, 1)))
    row_delta = jnp.sum(weighted * jnp.exp(tops - log_total), axis=(0, 1))
    pad = jnp.zeros((head_count, ROWS - dev_blocks - 1, tok_rows), jnp.float32)
    ld_slots = []
    for slot, shift in enumerate(shifts):
        per_block = jnp.where(allowed[slot], log_total[None], jnp.inf)
        ld = jnp.concatenate(
            [jnp.transpose(per_block, (1, 0, 2)), row_delta[:, None], pad], axis=1
        )
        ld_slots.append(ld if shift == 0 else from_behind(ld, "seq", -shift))
    out_q, out_kv = [], []
    for chunk in range(CHUNKS):
        dkv, *dq_parts = grad_call(
            kv_chunks[chunk], qg_by_chunk[chunk], ld_slots, chunk, chunk_heads
        )
        summed = dq_parts[OWN]
        for slot, shift in enumerate(shifts):
            if shift != 0:
                summed = summed + from_behind(dq_parts[slot], "seq", shift).astype(jnp.float32)
        out_q.append(summed.astype(jnp.bfloat16))
        out_kv.append(dkv)
    grad_kv = jnp.concatenate(out_kv, axis=2)
    return (jnp.concatenate(out_q, axis=1), grad_kv[0], grad_kv[1])


def solution(mesh):
    placed = (
        P(("group", "seq"), None),
        P(("group", "seq"), None),
        P(("group", "seq"), None),
        P(("group", "seq"), None),
        P(("group", "seq"), None),
        P(("group", "seq"), None),
    )
    return jax.shard_map(
        body,
        mesh=mesh,
        in_specs=placed,
        out_specs=(P(("group", "seq"), None), P(("group", "seq"), None), P(("group", "seq"), None)),
        check_vma=False,
    )
```

```python
import jax
import jax.numpy as jnp
from jax import lax
from jax.experimental import pallas as pl
from jax.experimental.pallas import tpu as pltpu
from jax.sharding import PartitionSpec as P

DH = 128
BLK = 128
CAMS = 4
SLOTS = 5
OWN = 2
ROWS = 8


LAST = (((1,), (1,)), ((), ()))
FIRST = (((0,), (0,)), ((), ()))


def from_behind(block, axis, distance):
    devices = range(lax.axis_size(axis))
    route = [((i - distance) % len(devices), i) for i in devices]
    return lax.ppermute(block, axis, route)


def block_allowed(view_rows, tile_rows, dev_blocks):
    joined = jnp.concatenate(
        [view_rows[:, :dev_blocks], tile_rows, view_rows[:, dev_blocks:]], axis=1
    )
    block_count = joined.shape[0]
    own_column = (
        2 * dev_blocks
        + lax.broadcasted_iota(jnp.int32, (block_count, 5 * dev_blocks), 0) % dev_blocks
    )
    column = lax.broadcasted_iota(jnp.int32, (block_count, 5 * dev_blocks), 1)
    return jnp.where(column == own_column, 1, joined)


def transposed_scores(kv_ref, qg_ref):
    score_scale = DH ** (-0.5)
    raw = lax.dot_general(kv_ref[0], qg_ref[0], LAST, preferred_element_type=jnp.float32)
    return raw * score_scale


def stats_kernel(kv_ref, *refs):
    qg_refs = refs[:SLOTS]
    stats_ref = refs[SLOTS]
    f32 = jnp.float32
    for slot in range(SLOTS):
        scores = transposed_scores(kv_ref, qg_refs[slot])
        grad_prob = lax.dot_general(kv_ref[1], qg_refs[slot][1], LAST, preferred_element_type=f32)
        rows = []
        for low in range(0, scores.shape[0], BLK):
            part = scores[low : low + BLK]
            top = jnp.max(part, axis=0, keepdims=True)
            weights = jnp.exp(part - top)
            total = jnp.sum(weights, axis=0, keepdims=True)
            weighted = jnp.sum(weights * grad_prob[low : low + BLK], axis=0, keepdims=True)
            rows += [top, total, weighted]
        pad = jnp.zeros((ROWS - len(rows), scores.shape[1]), f32)
        stats_ref[slot, 0] = jnp.concatenate(rows + [pad], axis=0)


def grad_kernel(kv_ref, *refs):
    qg_refs = refs[:SLOTS]
    ld_refs = refs[SLOTS : 2 * SLOTS]
    dkv_ref = refs[2 * SLOTS]
    dq_refs = refs[2 * SLOTS + 1 :]
    f32 = jnp.float32
    bf16 = jnp.bfloat16
    score_scale = DH ** (-0.5)
    acc_k = jnp.zeros(dkv_ref.shape[1:], f32)
    acc_v = jnp.zeros(dkv_ref.shape[1:], f32)
    for slot in range(SLOTS):
        scores = transposed_scores(kv_ref, qg_refs[slot])
        rows = ld_refs[slot][0]
        key_blocks = scores.shape[0] // BLK
        log_total = jnp.concatenate(
            [jnp.broadcast_to(rows[kb : kb + 1, :], (BLK, scores.shape[1])) for kb in range(key_blocks)],
            axis=0,
        )
        row_delta = rows[key_blocks : key_blocks + 1, :]
        prob_full = jnp.exp(scores - log_total)
        prob_half = prob_full.astype(bf16)
        grad_prob = lax.dot_general(kv_ref[1], qg_refs[slot][1], LAST, preferred_element_type=f32)
        grad_score = (prob_full * (grad_prob - row_delta)).astype(bf16)
        part_k = jnp.dot(grad_score, qg_refs[slot][0], preferred_element_type=f32) * score_scale
        part_v = jnp.dot(prob_half, qg_refs[slot][1], preferred_element_type=f32)
        acc_k = acc_k + part_k.astype(bf16).astype(f32)
        acc_v = acc_v + part_v.astype(bf16).astype(f32)
        part_q = lax.dot_general(grad_score, kv_ref[0], FIRST, preferred_element_type=f32)
        dq_refs[slot][...] = (part_q * score_scale).astype(dq_refs[slot].dtype)
    dkv_ref[0] = acc_k.astype(bf16)
    dkv_ref[1] = acc_v.astype(bf16)


def stats_call(kv, qg_slots, chunk_heads):
    rows = kv.shape[1]
    pair = pl.BlockSpec((2, rows, DH), lambda h: (0, 0, h))
    return pl.pallas_call(
        stats_kernel,
        grid=(chunk_heads,),
        in_specs=[pair] + [pair] * SLOTS,
        out_specs=pl.BlockSpec((SLOTS, 1, ROWS, rows), lambda h: (0, h, 0, 0)),
        out_shape=jax.ShapeDtypeStruct((SLOTS, chunk_heads, ROWS, rows), jnp.float32),
        compiler_params=pltpu.CompilerParams(vmem_limit_bytes=48 * 1024 * 1024),
    )(kv, *qg_slots)


def grad_call(kv, qg_slots, ld_slots, offset, head0, chunk_heads):
    rows = kv.shape[1]
    pair = pl.BlockSpec((2, rows, DH), lambda h: (0, 0, offset + h))
    out_pair = pl.BlockSpec((2, rows, DH), lambda h: (0, 0, h))
    ld_spec = pl.BlockSpec((1, ROWS, rows), lambda h: (head0 + h, 0, 0))
    row_spec = pl.BlockSpec((rows, DH), lambda h: (0, h))
    width = chunk_heads * DH
    dq_shapes = [
        jax.ShapeDtypeStruct((rows, width), jnp.float32 if slot == OWN else jnp.bfloat16)
        for slot in range(SLOTS)
    ]
    return pl.pallas_call(
        grad_kernel,
        grid=(chunk_heads,),
        in_specs=[pair] + [pair] * SLOTS + [ld_spec] * SLOTS,
        out_specs=[out_pair] + [row_spec] * SLOTS,
        out_shape=[jax.ShapeDtypeStruct((2, rows, width), jnp.bfloat16)] + dq_shapes,
        compiler_params=pltpu.CompilerParams(vmem_limit_bytes=48 * 1024 * 1024),
    )(kv, *qg_slots, *ld_slots)


def body(queries, keys, values, grad_out, view_mask, tile_mask):
    tok_rows, feature_width = queries.shape
    dev_blocks = tok_rows // BLK
    seq_size = lax.axis_size("seq")
    camera_span = seq_size // CAMS
    shifts = (camera_span, 1, 0, -1, -camera_span)
    blocks = block_allowed(view_mask, tile_mask, dev_blocks)
    allowed = jnp.repeat(blocks.T, BLK, axis=1).reshape(SLOTS, dev_blocks, 1, tok_rows) > 0
    head_count = feature_width // DH
    late_heads = max(head_count // 4, 1)
    spans = [(0, head_count - late_heads), (head_count - late_heads, late_heads)]

    def by_span(first, second, start, count):
        cols = slice(start * DH, (start + count) * DH)
        return jnp.stack([first[:, cols], second[:, cols]])

    kv_chunks = [by_span(keys, values, start, count) for start, count in spans]
    qg_by_chunk, stats_by_chunk = [], []
    for chunk, (start, count) in enumerate(spans):
        qg = by_span(queries, grad_out, start, count)
        qg_slots = [qg if shift == 0 else from_behind(qg, "seq", -shift) for shift in shifts]
        qg_by_chunk.append(qg_slots)
        stats_by_chunk.append(stats_call(kv_chunks[chunk], qg_slots, count))
    stats = jnp.concatenate(stats_by_chunk, axis=1)
    got = [
        stats[slot] if shift == 0 else from_behind(stats[slot], "seq", shift)
        for slot, shift in enumerate(shifts)
    ]
    got = jnp.stack(got)[:, :, : 3 * dev_blocks].reshape(
        SLOTS, head_count, dev_blocks, 3, tok_rows
    )
    got = jnp.transpose(got, (0, 2, 3, 1, 4))
    tops = jnp.where(allowed, got[:, :, 0], -jnp.inf)
    totals = jnp.where(allowed, got[:, :, 1], 0.0)
    weighted = jnp.where(allowed, got[:, :, 2], 0.0)
    overall = jnp.max(tops, axis=(0, 1))
    log_total = overall + jnp.log(jnp.sum(totals * jnp.exp(tops - overall), axis=(0, 1)))
    row_delta = jnp.sum(weighted * jnp.exp(tops - log_total), axis=(0, 1))
    pad = jnp.zeros((head_count, ROWS - dev_blocks - 1, tok_rows), jnp.float32)
    ld_slots = []
    for slot, shift in enumerate(shifts):
        per_block = jnp.where(allowed[slot], log_total[None], jnp.inf)
        ld = jnp.concatenate(
            [jnp.transpose(per_block, (1, 0, 2)), row_delta[:, None], pad], axis=1
        )
        ld_slots.append(ld if shift == 0 else from_behind(ld, "seq", -shift))
    early = spans[0][1]
    lead = min(late_heads, early)
    pieces = [(0, 0, lead), (0, lead, early - lead), (1, 0, late_heads)]
    out_q, out_kv = [], []
    for chunk, offset, count in pieces:
        if count == 0:
            continue
        dkv, *dq_parts = grad_call(
            kv_chunks[chunk], qg_by_chunk[chunk], ld_slots, offset, spans[chunk][0] + offset, count
        )
        summed = dq_parts[OWN]
        for slot, shift in enumerate(shifts):
            if shift != 0:
                summed = summed + from_behind(dq_parts[slot], "seq", shift).astype(jnp.float32)
        out_q.append(summed.astype(jnp.bfloat16))
        out_kv.append(dkv)
    grad_kv = jnp.concatenate(out_kv, axis=2)
    return (jnp.concatenate(out_q, axis=1), grad_kv[0], grad_kv[1])


def solution(mesh):
    placed = (
        P(("group", "seq"), None),
        P(("group", "seq"), None),
        P(("group", "seq"), None),
        P(("group", "seq"), None),
        P(("group", "seq"), None),
        P(("group", "seq"), None),
    )
    return jax.shard_map(
        body,
        mesh=mesh,
        in_specs=placed,
        out_specs=(P(("group", "seq"), None), P(("group", "seq"), None), P(("group", "seq"), None)),
        check_vma=False,
    )
```

```python
import jax
import jax.numpy as jnp
from jax import lax
from jax.experimental import pallas as pl
from jax.experimental.pallas import tpu as pltpu
from jax.sharding import PartitionSpec as P

DH = 128
BLK = 128
CAMS = 4
SLOTS = 5
OWN = 2
ROWS = 8


LAST = (((1,), (1,)), ((), ()))
FIRST = (((0,), (0,)), ((), ()))


def from_behind(block, axis, distance):
    devices = range(lax.axis_size(axis))
    route = [((i - distance) % len(devices), i) for i in devices]
    return lax.ppermute(block, axis, route)


def block_allowed(view_rows, tile_rows, dev_blocks):
    joined = jnp.concatenate(
        [view_rows[:, :dev_blocks], tile_rows, view_rows[:, dev_blocks:]], axis=1
    )
    block_count = joined.shape[0]
    own_column = (
        2 * dev_blocks
        + lax.broadcasted_iota(jnp.int32, (block_count, 5 * dev_blocks), 0) % dev_blocks
    )
    column = lax.broadcasted_iota(jnp.int32, (block_count, 5 * dev_blocks), 1)
    return jnp.where(column == own_column, 1, joined)


def transposed_scores(kv_ref, qg_ref):
    score_scale = DH ** (-0.5)
    raw = lax.dot_general(kv_ref[0], qg_ref[0], LAST, preferred_element_type=jnp.float32)
    return raw * score_scale


def stats_kernel(kv_ref, *refs):
    qg_refs = refs[:SLOTS]
    stats_ref = refs[SLOTS]
    f32 = jnp.float32
    for slot in range(SLOTS):
        scores = transposed_scores(kv_ref, qg_refs[slot])
        grad_prob = lax.dot_general(kv_ref[1], qg_refs[slot][1], LAST, preferred_element_type=f32)
        rows = []
        for low in range(0, scores.shape[0], BLK):
            part = scores[low : low + BLK]
            top = jnp.max(part, axis=0, keepdims=True)
            weights = jnp.exp(part - top)
            total = jnp.sum(weights, axis=0, keepdims=True)
            weighted = jnp.sum(weights * grad_prob[low : low + BLK], axis=0, keepdims=True)
            rows += [top, total, weighted]
        pad = jnp.zeros((ROWS - len(rows), scores.shape[1]), f32)
        stats_ref[slot, 0] = jnp.concatenate(rows + [pad], axis=0)


def grad_kernel(kv_ref, *refs):
    qg_refs = refs[:SLOTS]
    ld_refs = refs[SLOTS : 2 * SLOTS]
    dkv_ref = refs[2 * SLOTS]
    dq_refs = refs[2 * SLOTS + 1 :]
    f32 = jnp.float32
    bf16 = jnp.bfloat16
    score_scale = DH ** (-0.5)
    acc_k = jnp.zeros(dkv_ref.shape[1:], f32)
    acc_v = jnp.zeros(dkv_ref.shape[1:], f32)
    for slot in range(SLOTS):
        scores = transposed_scores(kv_ref, qg_refs[slot])
        rows = ld_refs[slot][0]
        key_blocks = scores.shape[0] // BLK
        log_total = jnp.concatenate(
            [jnp.broadcast_to(rows[kb : kb + 1, :], (BLK, scores.shape[1])) for kb in range(key_blocks)],
            axis=0,
        )
        row_delta = rows[key_blocks : key_blocks + 1, :]
        prob_full = jnp.exp(scores - log_total)
        prob_half = prob_full.astype(bf16)
        grad_prob = lax.dot_general(kv_ref[1], qg_refs[slot][1], LAST, preferred_element_type=f32)
        grad_score = (prob_full * (grad_prob - row_delta)).astype(bf16)
        part_k = jnp.dot(grad_score, qg_refs[slot][0], preferred_element_type=f32) * score_scale
        part_v = jnp.dot(prob_half, qg_refs[slot][1], preferred_element_type=f32)
        acc_k = acc_k + part_k.astype(bf16).astype(f32)
        acc_v = acc_v + part_v.astype(bf16).astype(f32)
        part_q = lax.dot_general(grad_score, kv_ref[0], FIRST, preferred_element_type=f32)
        dq_refs[slot][...] = (part_q * score_scale).astype(dq_refs[slot].dtype)
    dkv_ref[0] = acc_k.astype(bf16)
    dkv_ref[1] = acc_v.astype(bf16)


def stats_call(kv, qg_slots, chunk_heads):
    rows = kv.shape[1]
    pair = pl.BlockSpec((2, rows, DH), lambda h: (0, 0, h))
    return pl.pallas_call(
        stats_kernel,
        grid=(chunk_heads,),
        in_specs=[pair] + [pair] * SLOTS,
        out_specs=pl.BlockSpec((SLOTS, 1, ROWS, rows), lambda h: (0, h, 0, 0)),
        out_shape=jax.ShapeDtypeStruct((SLOTS, chunk_heads, ROWS, rows), jnp.float32),
        compiler_params=pltpu.CompilerParams(vmem_limit_bytes=48 * 1024 * 1024),
    )(kv, *qg_slots)


def grad_call(kv, qg_slots, ld_slots, offset, head0, chunk_heads):
    rows = kv.shape[1]
    pair = pl.BlockSpec((2, rows, DH), lambda h: (0, 0, offset + h))
    out_pair = pl.BlockSpec((2, rows, DH), lambda h: (0, 0, h))
    ld_spec = pl.BlockSpec((1, ROWS, rows), lambda h: (head0 + h, 0, 0))
    row_spec = pl.BlockSpec((rows, DH), lambda h: (0, h))
    width = chunk_heads * DH
    dq_shapes = [
        jax.ShapeDtypeStruct((rows, width), jnp.float32 if slot == OWN else jnp.bfloat16)
        for slot in range(SLOTS)
    ]
    return pl.pallas_call(
        grad_kernel,
        grid=(chunk_heads,),
        in_specs=[pair] + [pair] * SLOTS + [ld_spec] * SLOTS,
        out_specs=[out_pair] + [row_spec] * SLOTS,
        out_shape=[jax.ShapeDtypeStruct((2, rows, width), jnp.bfloat16)] + dq_shapes,
        compiler_params=pltpu.CompilerParams(vmem_limit_bytes=48 * 1024 * 1024),
    )(kv, *qg_slots, *ld_slots)


def body(queries, keys, values, grad_out, view_mask, tile_mask):
    tok_rows, feature_width = queries.shape
    dev_blocks = tok_rows // BLK
    seq_size = lax.axis_size("seq")
    camera_span = seq_size // CAMS
    shifts = (camera_span, 1, 0, -1, -camera_span)
    blocks = block_allowed(view_mask, tile_mask, dev_blocks)
    allowed = jnp.repeat(blocks.T, BLK, axis=1).reshape(SLOTS, dev_blocks, 1, tok_rows) > 0
    head_count = feature_width // DH
    late_heads = max(head_count // 4, 1)
    spans = [(0, late_heads), (late_heads, head_count - late_heads)]

    def by_span(first, second, start, count):
        cols = slice(start * DH, (start + count) * DH)
        return jnp.stack([first[:, cols], second[:, cols]])

    kv_chunks = [by_span(keys, values, start, count) for start, count in spans]
    qg_by_chunk = []
    for start, count in spans:
        qg = by_span(queries, grad_out, start, count)
        qg_by_chunk.append(
            [qg if shift == 0 else from_behind(qg, "seq", -shift) for shift in shifts]
        )
    late_stats = stats_call(kv_chunks[1], qg_by_chunk[1], spans[1][1])
    qg_by_chunk[0], _ = lax.optimization_barrier((qg_by_chunk[0], late_stats))
    stats_by_chunk = [stats_call(kv_chunks[0], qg_by_chunk[0], spans[0][1]), late_stats]
    stats = jnp.concatenate(stats_by_chunk, axis=1)
    got = [
        stats[slot] if shift == 0 else from_behind(stats[slot], "seq", shift)
        for slot, shift in enumerate(shifts)
    ]
    got = jnp.stack(got)[:, :, : 3 * dev_blocks].reshape(
        SLOTS, head_count, dev_blocks, 3, tok_rows
    )
    got = jnp.transpose(got, (0, 2, 3, 1, 4))
    tops = jnp.where(allowed, got[:, :, 0], -jnp.inf)
    totals = jnp.where(allowed, got[:, :, 1], 0.0)
    weighted = jnp.where(allowed, got[:, :, 2], 0.0)
    overall = jnp.max(tops, axis=(0, 1))
    log_total = overall + jnp.log(jnp.sum(totals * jnp.exp(tops - overall), axis=(0, 1)))
    row_delta = jnp.sum(weighted * jnp.exp(tops - log_total), axis=(0, 1))
    pad = jnp.zeros((head_count, ROWS - dev_blocks - 1, tok_rows), jnp.float32)
    ld_slots = []
    for slot, shift in enumerate(shifts):
        per_block = jnp.where(allowed[slot], log_total[None], jnp.inf)
        ld = jnp.concatenate(
            [jnp.transpose(per_block, (1, 0, 2)), row_delta[:, None], pad], axis=1
        )
        ld_slots.append(ld if shift == 0 else from_behind(ld, "seq", -shift))
    early = spans[1][1]
    lead = min(late_heads, early)
    pieces = [(0, 0, late_heads), (1, 0, lead), (1, lead, early - lead)]
    out_q, out_kv = [], []
    for chunk, offset, count in pieces:
        if count == 0:
            continue
        dkv, *dq_parts = grad_call(
            kv_chunks[chunk], qg_by_chunk[chunk], ld_slots, offset, spans[chunk][0] + offset, count
        )
        summed = dq_parts[OWN]
        for slot, shift in enumerate(shifts):
            if shift != 0:
                summed = summed + from_behind(dq_parts[slot], "seq", shift).astype(jnp.float32)
        out_q.append(summed.astype(jnp.bfloat16))
        out_kv.append(dkv)
    grad_kv = jnp.concatenate(out_kv, axis=2)
    return (jnp.concatenate(out_q, axis=1), grad_kv[0], grad_kv[1])


def solution(mesh):
    placed = (
        P(("group", "seq"), None),
        P(("group", "seq"), None),
        P(("group", "seq"), None),
        P(("group", "seq"), None),
        P(("group", "seq"), None),
        P(("group", "seq"), None),
    )
    return jax.shard_map(
        body,
        mesh=mesh,
        in_specs=placed,
        out_specs=(P(("group", "seq"), None), P(("group", "seq"), None), P(("group", "seq"), None)),
        check_vma=False,
    )
```

```python
import jax
import jax.numpy as jnp
from jax import lax
from jax.experimental import pallas as pl
from jax.experimental.pallas import tpu as pltpu
from jax.sharding import PartitionSpec as P

DH = 128
BLK = 128
CAMS = 4
SLOTS = 5
OWN = 2
ROWS = 8


LAST = (((1,), (1,)), ((), ()))
FIRST = (((0,), (0,)), ((), ()))


def from_behind(block, axis, distance):
    devices = range(lax.axis_size(axis))
    route = [((i - distance) % len(devices), i) for i in devices]
    return lax.ppermute(block, axis, route)


def block_allowed(view_rows, tile_rows, dev_blocks):
    joined = jnp.concatenate(
        [view_rows[:, :dev_blocks], tile_rows, view_rows[:, dev_blocks:]], axis=1
    )
    block_count = joined.shape[0]
    own_column = (
        2 * dev_blocks
        + lax.broadcasted_iota(jnp.int32, (block_count, 5 * dev_blocks), 0) % dev_blocks
    )
    column = lax.broadcasted_iota(jnp.int32, (block_count, 5 * dev_blocks), 1)
    return jnp.where(column == own_column, 1, joined)


def transposed_scores(kv_ref, qg_ref):
    score_scale = DH ** (-0.5)
    raw = lax.dot_general(kv_ref[0], qg_ref[0], LAST, preferred_element_type=jnp.float32)
    return raw * score_scale


def stats_kernel(kv_ref, *refs):
    qg_refs = refs[:SLOTS]
    stats_ref = refs[SLOTS]
    f32 = jnp.float32
    for slot in range(SLOTS):
        scores = transposed_scores(kv_ref, qg_refs[slot])
        grad_prob = lax.dot_general(kv_ref[1], qg_refs[slot][1], LAST, preferred_element_type=f32)
        rows = []
        for low in range(0, scores.shape[0], BLK):
            part = scores[low : low + BLK]
            top = jnp.max(part, axis=0, keepdims=True)
            weights = jnp.exp(part - top)
            total = jnp.sum(weights, axis=0, keepdims=True)
            weighted = jnp.sum(weights * grad_prob[low : low + BLK], axis=0, keepdims=True)
            rows += [top, total, weighted]
        pad = jnp.zeros((ROWS - len(rows), scores.shape[1]), f32)
        stats_ref[slot, 0] = jnp.concatenate(rows + [pad], axis=0)


def grad_kernel(kv_ref, *refs):
    qg_refs = refs[:SLOTS]
    ld_refs = refs[SLOTS : 2 * SLOTS]
    dkv_ref = refs[2 * SLOTS]
    dq_refs = refs[2 * SLOTS + 1 :]
    f32 = jnp.float32
    bf16 = jnp.bfloat16
    score_scale = DH ** (-0.5)
    acc_k = jnp.zeros(dkv_ref.shape[1:], f32)
    acc_v = jnp.zeros(dkv_ref.shape[1:], f32)
    for slot in range(SLOTS):
        scores = transposed_scores(kv_ref, qg_refs[slot])
        rows = ld_refs[slot][0]
        key_blocks = scores.shape[0] // BLK
        log_total = jnp.concatenate(
            [jnp.broadcast_to(rows[kb : kb + 1, :], (BLK, scores.shape[1])) for kb in range(key_blocks)],
            axis=0,
        )
        row_delta = rows[key_blocks : key_blocks + 1, :]
        prob_full = jnp.exp(scores - log_total)
        prob_half = prob_full.astype(bf16)
        grad_prob = lax.dot_general(kv_ref[1], qg_refs[slot][1], LAST, preferred_element_type=f32)
        grad_score = (prob_full * (grad_prob - row_delta)).astype(bf16)
        part_k = jnp.dot(grad_score, qg_refs[slot][0], preferred_element_type=f32) * score_scale
        part_v = jnp.dot(prob_half, qg_refs[slot][1], preferred_element_type=f32)
        acc_k = acc_k + part_k.astype(bf16).astype(f32)
        acc_v = acc_v + part_v.astype(bf16).astype(f32)
        part_q = lax.dot_general(grad_score, kv_ref[0], FIRST, preferred_element_type=f32)
        dq_refs[slot][...] = (part_q * score_scale).astype(dq_refs[slot].dtype)
    dkv_ref[0] = acc_k.astype(bf16)
    dkv_ref[1] = acc_v.astype(bf16)


def stats_call(kv, qg_slots, chunk_heads):
    rows = kv.shape[1]
    pair = pl.BlockSpec((2, rows, DH), lambda h: (0, 0, h))
    return pl.pallas_call(
        stats_kernel,
        grid=(chunk_heads,),
        in_specs=[pair] + [pair] * SLOTS,
        out_specs=pl.BlockSpec((SLOTS, 1, ROWS, rows), lambda h: (0, h, 0, 0)),
        out_shape=jax.ShapeDtypeStruct((SLOTS, chunk_heads, ROWS, rows), jnp.float32),
        compiler_params=pltpu.CompilerParams(vmem_limit_bytes=48 * 1024 * 1024),
    )(kv, *qg_slots)


def grad_call(kv, qg_slots, ld_slots, offset, head0, chunk_heads):
    rows = kv.shape[1]
    pair = pl.BlockSpec((2, rows, DH), lambda h: (0, 0, offset + h))
    out_pair = pl.BlockSpec((2, rows, DH), lambda h: (0, 0, h))
    ld_spec = pl.BlockSpec((1, ROWS, rows), lambda h: (head0 + h, 0, 0))
    row_spec = pl.BlockSpec((rows, DH), lambda h: (0, h))
    width = chunk_heads * DH
    dq_shapes = [
        jax.ShapeDtypeStruct((rows, width), jnp.float32 if slot == OWN else jnp.bfloat16)
        for slot in range(SLOTS)
    ]
    return pl.pallas_call(
        grad_kernel,
        grid=(chunk_heads,),
        in_specs=[pair] + [pair] * SLOTS + [ld_spec] * SLOTS,
        out_specs=[out_pair] + [row_spec] * SLOTS,
        out_shape=[jax.ShapeDtypeStruct((2, rows, width), jnp.bfloat16)] + dq_shapes,
        compiler_params=pltpu.CompilerParams(vmem_limit_bytes=48 * 1024 * 1024),
    )(kv, *qg_slots, *ld_slots)


def body(queries, keys, values, grad_out, view_mask, tile_mask):
    tok_rows, feature_width = queries.shape
    dev_blocks = tok_rows // BLK
    seq_size = lax.axis_size("seq")
    camera_span = seq_size // CAMS
    shifts = (camera_span, 1, 0, -1, -camera_span)
    blocks = block_allowed(view_mask, tile_mask, dev_blocks)
    allowed = jnp.repeat(blocks.T, BLK, axis=1).reshape(SLOTS, dev_blocks, 1, tok_rows) > 0
    head_count = feature_width // DH
    late_heads = max(head_count // 4, 1)
    spans = [(0, late_heads), (late_heads, head_count - late_heads)]

    def by_span(first, second, start, count):
        cols = slice(start * DH, (start + count) * DH)
        return jnp.stack([first[:, cols], second[:, cols]])

    kv_chunks = [by_span(keys, values, start, count) for start, count in spans]
    qg_by_chunk = []
    for start, count in spans:
        qg = by_span(queries, grad_out, start, count)
        qg_by_chunk.append(
            [qg if shift == 0 else from_behind(qg, "seq", -shift) for shift in shifts]
        )
    late_stats = stats_call(kv_chunks[1], qg_by_chunk[1], spans[1][1])
    qg_by_chunk[0], _ = lax.optimization_barrier((qg_by_chunk[0], late_stats))
    stats_by_chunk = [stats_call(kv_chunks[0], qg_by_chunk[0], spans[0][1]), late_stats]
    stats = jnp.concatenate(stats_by_chunk, axis=1)
    got = [
        stats[slot] if shift == 0 else from_behind(stats[slot], "seq", shift)
        for slot, shift in enumerate(shifts)
    ]
    got = jnp.stack(got)[:, :, : 3 * dev_blocks].reshape(
        SLOTS, head_count, dev_blocks, 3, tok_rows
    )
    got = jnp.transpose(got, (0, 2, 3, 1, 4))
    tops = jnp.where(allowed, got[:, :, 0], -jnp.inf)
    totals = jnp.where(allowed, got[:, :, 1], 0.0)
    weighted = jnp.where(allowed, got[:, :, 2], 0.0)
    overall = jnp.max(tops, axis=(0, 1))
    log_total = overall + jnp.log(jnp.sum(totals * jnp.exp(tops - overall), axis=(0, 1)))
    row_delta = jnp.sum(weighted * jnp.exp(tops - log_total), axis=(0, 1))
    pad = jnp.zeros((head_count, ROWS - dev_blocks - 1, tok_rows), jnp.float32)
    ld_slots = []
    for slot, shift in enumerate(shifts):
        per_block = jnp.where(allowed[slot], log_total[None], jnp.inf)
        ld = jnp.concatenate(
            [jnp.transpose(per_block, (1, 0, 2)), row_delta[:, None], pad], axis=1
        )
        ld_slots.append(ld if shift == 0 else from_behind(ld, "seq", -shift))
    early = spans[1][1]
    lead = min(late_heads, early)
    pieces = [(0, 0, late_heads), (1, 0, lead), (1, lead, early - lead)]
    out_q, out_kv = [], []
    previous = ()
    for chunk, offset, count in pieces:
        if count == 0:
            continue
        kv, qg_slots, ld_ready, _ = lax.optimization_barrier(
            (kv_chunks[chunk], qg_by_chunk[chunk], ld_slots, previous)
        )
        dkv, *dq_parts = grad_call(
            kv, qg_slots, ld_ready, offset, spans[chunk][0] + offset, count
        )
        previous = dkv
        summed = dq_parts[OWN]
        for slot, shift in enumerate(shifts):
            if shift != 0:
                summed = summed + from_behind(dq_parts[slot], "seq", shift).astype(jnp.float32)
        out_q.append(summed.astype(jnp.bfloat16))
        out_kv.append(dkv)
    grad_kv = jnp.concatenate(out_kv, axis=2)
    return (jnp.concatenate(out_q, axis=1), grad_kv[0], grad_kv[1])


def solution(mesh):
    placed = (
        P(("group", "seq"), None),
        P(("group", "seq"), None),
        P(("group", "seq"), None),
        P(("group", "seq"), None),
        P(("group", "seq"), None),
        P(("group", "seq"), None),
    )
    return jax.shard_map(
        body,
        mesh=mesh,
        in_specs=placed,
        out_specs=(P(("group", "seq"), None), P(("group", "seq"), None), P(("group", "seq"), None)),
        check_vma=False,
    )
```
